512 devices in a mesh: dp: 128 (over y, z, core), owner: 4 (over x).
Axes of the slice: x: 4, y: 8, z: 8, core: 2. Of those that a mesh axis runs over, the one named last changes fastest.
Arguments:
- embeddings: bfloat16 [65536, 1024], P(('dp', 'owner')), may hold values from -120 to 120
- assignment: int32 [65536], P(('dp', 'owner')), may hold values from 0 to 8191, as said below
- pair_list: int32 [8192], replicated, may hold values from 0 to 8191, as said below
Outputs:
- best_similarity: float32 [65536], P(('dp', 'owner'))
The draws below stay inside these ranges and needn't reach their ends.
Inputs may be any that keep to these rules, and one draw needn't show every extreme that they name: `assignment`: row r's cluster id is (t * n + o) * 16 + c, where n is the number of owner indices, o the owner index of the device holding row r, t an index of dp and c below 16. Among the rows of one device at most 2 share one t, and on every device exactly 2 rows share some t. pair_list[pair_list[k]] = k for every cluster k; cluster k = (t * n + o) * 16 + c and its partner have the same t and different owner indices o.
All inputs are finite; a program needn't handle non-finite values.
Results may differ from the reference program's by a relative error of at most 0.00053.
Values may be sent and summed in bfloat16 or wider, within the bound.
No kernel may reach another device: no remote copies, remote signals or barrier semaphores. Data moves between devices by JAX's collectives and lax.ppermute only.
A program may use at most 64 MiB of HBM per device.

```python
import jax
import jax.numpy as jnp
from jax import lax

D = 1024
ROW_DEV = 128
CPD = 16
CAP = 2
SLOTS = 256
ROWS = 65536
NCL = 8192
N_DP = 128
N_OWNER = 4


def layout_draw(key):
    pair_key = jax.random.fold_in(key, 11)
    perm_key, xor_key = jax.random.split(pair_key)
    perms = jax.vmap(lambda k: jax.random.permutation(k, CPD))(jax.random.split(perm_key, N_DP * N_OWNER))
    perms = perms.reshape(N_DP, N_OWNER, CPD).astype(jnp.int32)
    xors = jax.random.randint(xor_key, (N_DP, CPD), 1, N_OWNER).astype(jnp.int32)
    owners = jnp.arange(N_OWNER, dtype=jnp.int32)
    dps = jnp.arange(N_DP, dtype=jnp.int32)
    peer = jnp.bitwise_xor(owners[None, :, None], xors[:, None, :])
    peer_local = jnp.take_along_axis(perms, peer, axis=1)
    partner_id = (dps[:, None, None] * N_OWNER + peer) * CPD + peer_local
    own_id = (dps[:, None, None] * N_OWNER + owners[None, :, None]) * CPD + perms
    pairs = jnp.zeros((NCL,), jnp.int32).at[own_id.reshape(-1)].set(partner_id.reshape(-1))
    row_key = jax.random.fold_in(key, 12)
    spike_key, pick_key, order_key, local_key = jax.random.split(row_key, 4)
    devices = N_DP * N_OWNER
    spike = jax.random.randint(spike_key, (devices,), 0, N_DP).astype(jnp.int32)
    picks = jax.vmap(lambda k: jax.random.permutation(k, (N_DP - 1) * CAP))(jax.random.split(pick_key, devices))
    picks = picks[:, :ROW_DEV - CAP].astype(jnp.int32)
    heads = jnp.broadcast_to(spike[:, None], (devices, CAP))
    others = (spike[:, None] + 1 + picks // CAP) % N_DP
    dest_list = jnp.concatenate([heads, others], axis=1)
    order = jax.vmap(lambda k: jax.random.permutation(k, ROW_DEV))(jax.random.split(order_key, devices)).astype(jnp.int32)
    dest = jnp.take_along_axis(dest_list, order, axis=1)
    local = jax.random.randint(local_key, (devices, ROW_DEV), 0, CPD).astype(jnp.int32)
    owner_of = (jnp.arange(devices, dtype=jnp.int32) % N_OWNER)[:, None]
    assign = ((dest * N_OWNER + owner_of) * CPD + local).reshape(-1)
    return (assign, pairs)


def draw_assignment(key, part):
    assign, pairs = layout_draw(key)
    return assign


def draw_pair_list(key, part):
    assign, pairs = layout_draw(key)
    return pairs


def draw_embeddings(key, part):
    assign, pairs = layout_draw(key)
    emb_key = jax.random.fold_in(key, 13)
    base_key, own_key, amp_key, noise_key = jax.random.split(emb_key, 4)
    base = jax.random.truncated_normal(base_key, -4.0, 4.0, (NCL, D), jnp.float32)
    own = jax.random.truncated_normal(own_key, -4.0, 4.0, (NCL, D), jnp.float32)
    anchor = jnp.minimum(assign, jnp.take(pairs, assign))
    amp = jax.random.uniform(amp_key, (ROWS, 1), jnp.float32, 0.2, 1.4)
    noise = jax.random.truncated_normal(noise_key, -4.0, 4.0, (ROWS, D), jnp.float32)
    values = amp * (0.9 * jnp.take(base, anchor, axis=0) + 0.436 * jnp.take(own, assign, axis=0)) + noise
    return values.astype(jnp.bfloat16)


def setup_inputs(seed: int = 0) -> dict:
    key_of = jax.random.split(jax.random.key(seed), 4)
    return {
        "embeddings": draw_embeddings(jax.random.fold_in(key_of[3], 71), 0),
        "assignment": draw_assignment(jax.random.fold_in(key_of[3], 71), 0),
        "pair_list": draw_pair_list(jax.random.fold_in(key_of[3], 71), 0),
    }


def reference(embeddings, assignment, pair_list):
    values = embeddings.astype(jnp.float32)
    unit = (values * lax.rsqrt(lax.optimization_barrier(jnp.sum(values * values, axis=1, keepdims=True)) + 1e-06)).astype(jnp.bfloat16)
    devices = N_DP * N_OWNER
    target = assignment // (N_OWNER * CPD)
    by_device = target.reshape(devices, ROW_DEV)
    onehot = (by_device[:, :, None] == jnp.arange(N_DP, dtype=jnp.int32)[None, None, :]).astype(jnp.int32)
    slot = (lax.optimization_barrier(jnp.sum(jnp.cumsum(onehot, axis=1) * onehot, axis=2)) - 1).reshape(-1)
    source = jnp.arange(ROWS, dtype=jnp.int32) // ROW_DEV
    source_dp = source // N_OWNER
    source_owner = source % N_OWNER
    flat = (((target * N_OWNER + source_owner) * N_DP + source_dp) * CAP + slot).astype(jnp.int32)
    table = jnp.zeros((N_DP * N_OWNER * SLOTS, D), jnp.bfloat16).at[flat].set(unit)
    table = table.reshape(N_DP, N_OWNER, SLOTS, D)
    table_ids = jnp.full((N_DP * N_OWNER * SLOTS,), -1, jnp.int32).at[flat].set(assignment)
    table_ids = table_ids.reshape(N_DP, N_OWNER, SLOTS)

    def group(item):
        rows_t, ids_t = item
        every_row = rows_t.reshape(N_OWNER * SLOTS, D)
        every_id = ids_t.reshape(N_OWNER * SLOTS)
        column = jnp.arange(N_OWNER * SLOTS, dtype=jnp.int32)

        def one_owner(owner_index):
            mine = rows_t[owner_index]
            mine_ids = ids_t[owner_index]
            partner = jnp.take(pair_list, jnp.maximum(mine_ids, 0))
            scores = jnp.dot(mine.astype(jnp.float32), every_row.astype(jnp.float32).T)
            itself = owner_index * SLOTS + jnp.arange(SLOTS, dtype=jnp.int32)
            same = (mine_ids[:, None] == every_id[None, :]) & (every_id[None, :] >= 0) & (itself[:, None] != column[None, :])
            related = same | (partner[:, None] == every_id[None, :])
            return jnp.maximum(-1.0, lax.optimization_barrier(jnp.max(jnp.where(related, scores, -1.0), axis=1)))
        return lax.map(one_owner, jnp.arange(N_OWNER, dtype=jnp.int32))
    best = lax.map(group, (table, table_ids))
    return best.reshape(-1)[flat]
```

```python
import jax
import jax.numpy as jnp
from jax import lax
from jax.sharding import PartitionSpec as P

CPD = 16


def shards(embeddings, assignment, pair_list):
    rows, width = embeddings.shape
    n_dp = lax.axis_size("dp")
    n_owner = lax.axis_size("owner")
    capacity = 2 * rows // n_dp
    slots = capacity * n_dp
    here_owner = lax.axis_index("owner")
    here_dp = lax.axis_index("dp")

    all_ids = lax.all_gather(assignment, ("dp", "owner"), axis=0, tiled=False)
    all_ids = all_ids.reshape(n_dp, n_owner, rows)

    values = embeddings.astype(jnp.float32)
    unit = (values * lax.rsqrt(jnp.sum(values * values, axis=1, keepdims=True) + 1e-06)).astype(
        jnp.bfloat16
    )
    target = assignment // (n_owner * CPD)
    onehot = (target[:, None] == jnp.arange(n_dp, dtype=jnp.int32)[None, :]).astype(jnp.int32)
    slot = jnp.sum(jnp.cumsum(onehot, axis=0) * onehot, axis=1) - 1
    position = target * capacity + slot
    first_id = (here_dp * n_owner + here_owner) * CPD
    partners_mine = lax.dynamic_slice_in_dim(pair_list, first_id, CPD)
    send_rows = jnp.zeros((slots, width), jnp.bfloat16).at[position].set(unit)
    got_rows = lax.all_to_all(
        send_rows.reshape(n_dp, capacity, width), "dp", split_axis=0, concat_axis=0, tiled=True
    )
    mine = got_rows.reshape(slots, width)
    rows_p = lax.all_gather(mine, "owner", axis=0, tiled=True)

    hit = (all_ids // (n_owner * CPD)) == here_dp
    rank = jnp.cumsum(hit.astype(jnp.int32), axis=2) - 1
    which = hit[:, :, :, None] & (
        rank[:, :, :, None] == jnp.arange(capacity, dtype=jnp.int32)[None, None, None, :]
    )
    filled = jnp.any(which, axis=2)
    table = jnp.sum(jnp.where(which, all_ids[:, :, :, None], 0), axis=2)
    table = jnp.where(filled, table, -1)
    ids_p = jnp.transpose(table, (1, 0, 2)).reshape(n_owner * slots)
    mine_ids = lax.dynamic_slice_in_dim(ids_p, here_owner * slots, slots)

    local = jnp.clip(mine_ids - first_id, 0, CPD - 1)
    picked = local[:, None] == jnp.arange(CPD, dtype=jnp.int32)[None, :]
    partner = jnp.sum(jnp.where(picked, partners_mine[None, :], 0), axis=1)
    scores = lax.dot_general(
        mine, rows_p, (((1,), (1,)), ((), ())), preferred_element_type=jnp.float32
    )
    column = jnp.arange(ids_p.shape[0], dtype=jnp.int32)
    itself = here_owner * slots + jnp.arange(slots, dtype=jnp.int32)
    same = (
        (mine_ids[:, None] == ids_p[None, :])
        & (ids_p[None, :] >= 0)
        & (itself[:, None] != column[None, :])
    )
    related = same | (partner[:, None] == ids_p[None, :])
    best = jnp.maximum(-1.0, jnp.max(jnp.where(related, scores, -1.0), axis=1))
    every_best = lax.all_gather(best, "dp", axis=0, tiled=True)
    back = target * slots + here_dp * capacity + slot
    return jnp.take(every_best, back)


def solution(mesh):
    placed = (P(("dp", "owner"), None), P(("dp", "owner")), P())
    return jax.shard_map(
        shards, mesh=mesh, in_specs=placed, out_specs=P(("dp", "owner")), check_vma=False
    )
```

```python
import jax
import jax.numpy as jnp
from jax import lax
from jax.sharding import PartitionSpec as P

CPD = 16
LANES = 128


def shards(embeddings, assignment, pair_list):
    rows, width = embeddings.shape
    n_dp = lax.axis_size("dp")
    n_owner = lax.axis_size("owner")
    capacity = 2 * rows // n_dp
    slots = capacity * n_dp
    here_owner = lax.axis_index("owner")
    here_dp = lax.axis_index("dp")
    values = embeddings.astype(jnp.float32)
    unit = (values * lax.rsqrt(jnp.sum(values * values, axis=1, keepdims=True) + 1e-06)).astype(
        jnp.bfloat16
    )
    target = assignment // (n_owner * CPD)
    onehot = (target[:, None] == jnp.arange(n_dp, dtype=jnp.int32)[None, :]).astype(jnp.int32)
    slot = jnp.sum(jnp.cumsum(onehot, axis=0) * onehot, axis=1) - 1
    position = target * capacity + slot
    first_id = (here_dp * n_owner + here_owner) * CPD
    partners_mine = lax.dynamic_slice_in_dim(pair_list, first_id, CPD)

    code = (assignment % CPD + 1).astype(jnp.bfloat16)
    lane = jnp.arange(LANES, dtype=jnp.int32)
    extra = jnp.where(lane[None, :] == 0, code[:, None], jnp.zeros((), jnp.bfloat16))
    packed = jnp.concatenate([unit, extra], axis=1)
    send = jnp.zeros((slots, width + LANES), jnp.bfloat16).at[position].set(packed)
    got = lax.all_to_all(
        send.reshape(n_dp, capacity, width + LANES), "dp", split_axis=0, concat_axis=0, tiled=True
    ).reshape(slots, width + LANES)

    blocks = [got]
    for k in range(1, n_owner):
        blocks.append(
            lax.ppermute(got, "owner", [(i, (i + k) % n_owner) for i in range(n_owner)])
        )

    def ids_of(block, k):
        c1 = block[:, width].astype(jnp.int32)
        owner_k = (here_owner - k) % n_owner
        return jnp.where(c1 > 0, (here_dp * n_owner + owner_k) * CPD + c1 - 1, -1)

    mine = got[:, :width]
    mine_ids = ids_of(got, 0)
    local = jnp.clip(mine_ids - first_id, 0, CPD - 1)
    picked = local[:, None] == jnp.arange(CPD, dtype=jnp.int32)[None, :]
    partner = jnp.sum(jnp.where(picked, partners_mine[None, :], 0), axis=1)
    itself = jnp.arange(slots, dtype=jnp.int32)
    best = jnp.full((slots,), -1.0, jnp.float32)
    for k, block in enumerate(blocks):
        ids_k = ids_of(block, k)
        scores = lax.dot_general(
            mine, block[:, :width], (((1,), (1,)), ((), ())), preferred_element_type=jnp.float32
        )
        same = (mine_ids[:, None] == ids_k[None, :]) & (ids_k[None, :] >= 0)
        if k == 0:
            same = same & (itself[:, None] != itself[None, :])
        related = same | (partner[:, None] == ids_k[None, :])
        best = jnp.maximum(best, jnp.max(jnp.where(related, scores, -1.0), axis=1))
    returned = lax.all_to_all(
        best.reshape(n_dp, capacity), "dp", split_axis=0, concat_axis=0, tiled=True
    )
    return returned.reshape(slots)[position]


def solution(mesh):
    placed = (P(("dp", "owner"), None), P(("dp", "owner")), P())
    return jax.shard_map(
        shards, mesh=mesh, in_specs=placed, out_specs=P(("dp", "owner")), check_vma=False
    )
```

```python
import jax
import jax.numpy as jnp
from jax import lax
from jax.sharding import PartitionSpec as P

CPD = 16
LANES = 128


def shards(embeddings, assignment, pair_list):
    rows, width = embeddings.shape
    n_dp = lax.axis_size("dp")
    n_owner = lax.axis_size("owner")
    assert n_owner == 4
    capacity = 2 * rows // n_dp
    slots = capacity * n_dp
    here_owner = lax.axis_index("owner")
    here_dp = lax.axis_index("dp")
    values = embeddings.astype(jnp.float32)
    unit = (values * lax.rsqrt(jnp.sum(values * values, axis=1, keepdims=True) + 1e-06)).astype(
        jnp.bfloat16
    )
    target = assignment // (n_owner * CPD)
    onehot = (target[:, None] == jnp.arange(n_dp, dtype=jnp.int32)[None, :]).astype(jnp.int32)
    slot = jnp.sum(jnp.cumsum(onehot, axis=0) * onehot, axis=1) - 1
    position = target * capacity + slot
    first_id = (here_dp * n_owner + here_owner) * CPD

    code = (assignment % CPD + 1).astype(jnp.bfloat16)
    lane = jnp.arange(LANES, dtype=jnp.int32)
    extra = jnp.where(lane[None, :] == 0, code[:, None], jnp.zeros((), jnp.bfloat16))
    packed = jnp.concatenate([unit, extra], axis=1)
    send = jnp.zeros((slots, width + LANES), jnp.bfloat16).at[position].set(packed)
    got = lax.all_to_all(
        send.reshape(n_dp, capacity, width + LANES), "dp", split_axis=0, concat_axis=0, tiled=True
    ).reshape(slots, width + LANES)

    mine = got[:, :width]
    c1 = got[:, width].astype(jnp.int32)
    mine_ids = jnp.where(c1 > 0, first_id + c1 - 1, -1)

    to_next = [(i, (i + 1) % n_owner) for i in range(n_owner)]
    to_prev = [(i, (i - 1) % n_owner) for i in range(n_owner)]
    rows_l = lax.ppermute(mine, "owner", to_next)
    ids_l = lax.ppermute(mine_ids, "owner", to_next)
    rows_r = lax.ppermute(mine, "owner", to_prev)
    ids_r = lax.ppermute(mine_ids, "owner", to_prev)

    def partner_of(ids, owner_index):
        base = (here_dp * n_owner + owner_index) * CPD
        partners = lax.dynamic_slice_in_dim(pair_list, base, CPD)
        local = jnp.clip(ids - base, 0, CPD - 1)
        picked = local[:, None] == jnp.arange(CPD, dtype=jnp.int32)[None, :]
        return jnp.sum(jnp.where(picked, partners[None, :], 0), axis=1)

    def best_against(rows_a, ids_a, partner_a, rows_b, ids_b, itself):
        scores = lax.dot_general(
            rows_a, rows_b, (((1,), (1,)), ((), ())), preferred_element_type=jnp.float32
        )
        same = (ids_a[:, None] == ids_b[None, :]) & (ids_b[None, :] >= 0)
        if itself:
            column = jnp.arange(slots, dtype=jnp.int32)
            same = same & (column[:, None] != column[None, :])
        related = same | (partner_a[:, None] == ids_b[None, :])
        return jnp.max(jnp.where(related, scores, -1.0), axis=1)

    partner = partner_of(mine_ids, here_owner)
    partner_l = partner_of(ids_l, (here_owner - 1) % n_owner)
    far = best_against(rows_l, ids_l, partner_l, rows_r, ids_r, False)
    far_back = lax.ppermute(far, "owner", to_prev)
    best = jnp.maximum(
        jnp.maximum(-1.0, best_against(mine, mine_ids, partner, mine, mine_ids, True)),
        jnp.maximum(
            best_against(mine, mine_ids, partner, rows_l, ids_l, False),
            best_against(mine, mine_ids, partner, rows_r, ids_r, False),
        ),
    )
    best = jnp.maximum(best, far_back)
    returned = lax.all_to_all(
        best.reshape(n_dp, capacity), "dp", split_axis=0, concat_axis=0, tiled=True
    )
    return returned.reshape(slots)[position]


def solution(mesh):
    placed = (P(("dp", "owner"), None), P(("dp", "owner")), P())
    return jax.shard_map(
        shards, mesh=mesh, in_specs=placed, out_specs=P(("dp", "owner")), check_vma=False
    )
```

```python
import jax
import jax.numpy as jnp
from jax import lax
from jax.sharding import PartitionSpec as P

CPD = 16
LANES = 128


def shards(embeddings, assignment, pair_list):
    rows, width = embeddings.shape
    n_dp = lax.axis_size("dp")
    n_owner = lax.axis_size("owner")
    assert n_owner == 4
    capacity = 2 * rows // n_dp
    slots = capacity * n_dp
    here_owner = lax.axis_index("owner")
    here_dp = lax.axis_index("dp")
    values = embeddings.astype(jnp.float32)
    unit = (values * lax.rsqrt(jnp.sum(values * values, axis=1, keepdims=True) + 1e-06)).astype(
        jnp.bfloat16
    )
    target = assignment // (n_owner * CPD)
    onehot = (target[:, None] == jnp.arange(n_dp, dtype=jnp.int32)[None, :]).astype(jnp.int32)
    slot = jnp.sum(jnp.cumsum(onehot, axis=0) * onehot, axis=1) - 1
    position = target * capacity + slot
    first_id = (here_dp * n_owner + here_owner) * CPD

    code = (assignment % CPD + 1).astype(jnp.bfloat16)
    lane = jnp.arange(LANES, dtype=jnp.int32)
    extra = jnp.where(lane[None, :] == 0, code[:, None], jnp.zeros((), jnp.bfloat16))
    packed = jnp.concatenate([unit, extra], axis=1)
    send = jnp.zeros((n_dp, capacity, width + LANES), jnp.bfloat16).at[target, slot].set(packed)
    got = lax.all_to_all(send, "dp", split_axis=0, concat_axis=0, tiled=True).reshape(
        slots, width + LANES
    )

    mine = got[:, :width]
    c1 = got[:, width].astype(jnp.int32)
    mine_ids = jnp.where(c1 > 0, first_id + c1 - 1, -1)

    to_next = [(i, (i + 1) % n_owner) for i in range(n_owner)]
    to_prev = [(i, (i - 1) % n_owner) for i in range(n_owner)]
    got_l = lax.ppermute(got, "owner", to_next)
    got_r = lax.ppermute(got, "owner", to_prev)

    def ids_of(block, owner_index):
        c1 = block[:, width].astype(jnp.int32)
        return jnp.where(c1 > 0, (here_dp * n_owner + owner_index) * CPD + c1 - 1, -1)

    rows_l = got_l[:, :width]
    ids_l = ids_of(got_l, (here_owner - 1) % n_owner)
    rows_r = got_r[:, :width]
    ids_r = ids_of(got_r, (here_owner + 1) % n_owner)

    def partner_of(ids, owner_index):
        base = (here_dp * n_owner + owner_index) * CPD
        partners = lax.dynamic_slice_in_dim(pair_list, base, CPD)
        local = jnp.clip(ids - base, 0, CPD - 1)
        picked = local[:, None] == jnp.arange(CPD, dtype=jnp.int32)[None, :]
        return jnp.sum(jnp.where(picked, partners[None, :], 0), axis=1)

    def best_against(rows_a, ids_a, partner_a, rows_b, ids_b, itself):
        scores = lax.dot_general(
            rows_a, rows_b, (((1,), (1,)), ((), ())), preferred_element_type=jnp.float32
        )
        same = (ids_a[:, None] == ids_b[None, :]) & (ids_b[None, :] >= 0)
        if itself:
            column = jnp.arange(slots, dtype=jnp.int32)
            same = same & (column[:, None] != column[None, :])
        related = same | (partner_a[:, None] == ids_b[None, :])
        return jnp.max(jnp.where(related, scores, -1.0), axis=1)

    partner = partner_of(mine_ids, here_owner)
    partner_l = partner_of(ids_l, (here_owner - 1) % n_owner)
    far = best_against(rows_l, ids_l, partner_l, rows_r, ids_r, False)
    far_back = lax.ppermute(far, "owner", to_prev)
    best = jnp.maximum(
        jnp.maximum(-1.0, best_against(mine, mine_ids, partner, mine, mine_ids, True)),
        jnp.maximum(
            best_against(mine, mine_ids, partner, rows_l, ids_l, False),
            best_against(mine, mine_ids, partner, rows_r, ids_r, False),
        ),
    )
    best = jnp.maximum(best, far_back)
    returned = lax.all_to_all(
        best.reshape(n_dp, capacity), "dp", split_axis=0, concat_axis=0, tiled=True
    )
    pick = position[:, None] == jnp.arange(slots, dtype=jnp.int32)[None, :]
    return jnp.sum(jnp.where(pick, returned.reshape(slots)[None, :], 0.0), axis=1)


def solution(mesh):
    placed = (P(("dp", "owner"), None), P(("dp", "owner")), P())
    return jax.shard_map(
        shards, mesh=mesh, in_specs=placed, out_specs=P(("dp", "owner")), check_vma=False
    )
```

```python
import jax
import jax.numpy as jnp
from jax import lax
from jax.sharding import PartitionSpec as P

CPD = 16
LANES = 128


def shards(embeddings, assignment, pair_list):
    rows, width = embeddings.shape
    n_dp = lax.axis_size("dp")
    n_owner = lax.axis_size("owner")
    assert n_owner == 4
    capacity = 2 * rows // n_dp
    slots = capacity * n_dp
    here_owner = lax.axis_index("owner")
    here_dp = lax.axis_index("dp")
    values = embeddings.astype(jnp.float32)
    unit = (values * lax.rsqrt(jnp.sum(values * values, axis=1, keepdims=True) + 1e-06)).astype(
        jnp.bfloat16
    )
    target = assignment // (n_owner * CPD)
    onehot = (target[:, None] == jnp.arange(n_dp, dtype=jnp.int32)[None, :]).astype(jnp.int32)
    slot = jnp.sum(jnp.cumsum(onehot, axis=0) * onehot, axis=1) - 1
    position = target * capacity + slot
    first_id = (here_dp * n_owner + here_owner) * CPD

    code = (assignment % CPD + 1).astype(jnp.bfloat16)
    lane = jnp.arange(LANES, dtype=jnp.int32)
    extra = jnp.where(lane[None, :] == 0, code[:, None], jnp.zeros((), jnp.bfloat16))
    packed = jnp.concatenate([unit, extra], axis=1)
    place = (target[None, None, :] == jnp.arange(n_dp, dtype=jnp.int32)[:, None, None]) & (
        slot[None, None, :] == jnp.arange(capacity, dtype=jnp.int32)[None, :, None]
    )
    send = jnp.einsum(
        "tkr,rw->tkw", place.astype(jnp.bfloat16), packed, preferred_element_type=jnp.float32
    ).astype(jnp.bfloat16)
    got = lax.all_to_all(send, "dp", split_axis=0, concat_axis=0, tiled=True).reshape(
        slots, width + LANES
    )

    mine = got[:, :width]
    c1 = got[:, width].astype(jnp.int32)
    mine_ids = jnp.where(c1 > 0, first_id + c1 - 1, -1)

    to_next = [(i, (i + 1) % n_owner) for i in range(n_owner)]
    to_prev = [(i, (i - 1) % n_owner) for i in range(n_owner)]
    got_l = lax.ppermute(got, "owner", to_next)
    got_r = lax.ppermute(got, "owner", to_prev)

    def ids_of(block, owner_index):
        c1 = block[:, width].astype(jnp.int32)
        return jnp.where(c1 > 0, (here_dp * n_owner + owner_index) * CPD + c1 - 1, -1)

    rows_l = got_l[:, :width]
    ids_l = ids_of(got_l, (here_owner - 1) % n_owner)
    rows_r = got_r[:, :width]
    ids_r = ids_of(got_r, (here_owner + 1) % n_owner)

    def partner_of(ids, owner_index):
        base = (here_dp * n_owner + owner_index) * CPD
        partners = lax.dynamic_slice_in_dim(pair_list, base, CPD)
        local = jnp.clip(ids - base, 0, CPD - 1)
        picked = local[:, None] == jnp.arange(CPD, dtype=jnp.int32)[None, :]
        return jnp.sum(jnp.where(picked, partners[None, :], 0), axis=1)

    def best_against(rows_a, ids_a, partner_a, rows_b, ids_b, itself):
        scores = lax.dot_general(
            rows_a, rows_b, (((1,), (1,)), ((), ())), preferred_element_type=jnp.float32
        )
        same = (ids_a[:, None] == ids_b[None, :]) & (ids_b[None, :] >= 0)
        if itself:
            column = jnp.arange(slots, dtype=jnp.int32)
            same = same & (column[:, None] != column[None, :])
        related = same | (partner_a[:, None] == ids_b[None, :])
        return jnp.max(jnp.where(related, scores, -1.0), axis=1)

    partner = partner_of(mine_ids, here_owner)
    partner_l = partner_of(ids_l, (here_owner - 1) % n_owner)
    far = best_against(rows_l, ids_l, partner_l, rows_r, ids_r, False)
    far_back = lax.ppermute(far, "owner", to_prev)
    best = jnp.maximum(
        jnp.maximum(-1.0, best_against(mine, mine_ids, partner, mine, mine_ids, True)),
        jnp.maximum(
            best_against(mine, mine_ids, partner, rows_l, ids_l, False),
            best_against(mine, mine_ids, partner, rows_r, ids_r, False),
        ),
    )
    best = jnp.maximum(best, far_back)
    wide = jnp.pad(best.reshape(n_dp, capacity), ((0, 0), (0, LANES - capacity)))
    returned = lax.all_to_all(wide, "dp", split_axis=0, concat_axis=0, tiled=True)
    returned = returned[:, :capacity].reshape(slots)
    pick = position[:, None] == jnp.arange(slots, dtype=jnp.int32)[None, :]
    return jnp.sum(jnp.where(pick, returned[None, :], 0.0), axis=1)


def solution(mesh):
    placed = (P(("dp", "owner"), None), P(("dp", "owner")), P())
    return jax.shard_map(
        shards, mesh=mesh, in_specs=placed, out_specs=P(("dp", "owner")), check_vma=False
    )
```

```python
import jax
import jax.numpy as jnp
from jax import lax
from jax.sharding import PartitionSpec as P

CPD = 16
LANES = 128


def shards(embeddings, assignment, pair_list):
    rows, width = embeddings.shape
    n_dp = lax.axis_size("dp")
    n_owner = lax.axis_size("owner")
    assert n_owner == 4
    capacity = 2 * rows // n_dp
    slots = capacity * n_dp
    here_owner = lax.axis_index("owner")
    here_dp = lax.axis_index("dp")
    values = embeddings.astype(jnp.float32)
    scale = lax.rsqrt(jnp.sum(values * values, axis=1) + 1e-06)
    target = assignment // (n_owner * CPD)
    order = jnp.arange(rows, dtype=jnp.int32)
    earlier = (target[:, None] == target[None, :]) & (order[None, :] < order[:, None])
    slot = jnp.sum(earlier.astype(jnp.int32), axis=1)
    position = target * capacity + slot
    first_id = (here_dp * n_owner + here_owner) * CPD

    code = (assignment % CPD + 1).astype(jnp.bfloat16)
    lane = jnp.arange(LANES, dtype=jnp.int32)
    extra = jnp.where(lane[None, :] == 0, code[:, None], jnp.zeros((), jnp.bfloat16))
    packed = jnp.concatenate([embeddings, extra], axis=1)
    place = (target[None, None, :] == jnp.arange(n_dp, dtype=jnp.int32)[:, None, None]) & (
        slot[None, None, :] == jnp.arange(capacity, dtype=jnp.int32)[None, :, None]
    )
    moved = jnp.einsum(
        "tkr,rw->tkw", place.astype(jnp.bfloat16), packed, preferred_element_type=jnp.float32
    )
    slot_scale = jnp.sum(jnp.where(place, scale[None, None, :], 0.0), axis=2)
    lanes_all = jnp.arange(width + LANES, dtype=jnp.int32)
    send = jnp.where(
        lanes_all[None, None, :] < width, moved * slot_scale[:, :, None], moved
    ).astype(jnp.bfloat16)
    got = lax.all_to_all(send, "dp", split_axis=0, concat_axis=0, tiled=True).reshape(
        slots, width + LANES
    )

    mine = got[:, :width]
    c1 = got[:, width].astype(jnp.int32)
    mine_ids = jnp.where(c1 > 0, first_id + c1 - 1, -1)

    to_next = [(i, (i + 1) % n_owner) for i in range(n_owner)]
    to_prev = [(i, (i - 1) % n_owner) for i in range(n_owner)]
    got_l = lax.ppermute(got, "owner", to_next)
    got_r = lax.ppermute(got, "owner", to_prev)

    def ids_of(block, owner_index):
        c1 = block[:, width].astype(jnp.int32)
        return jnp.where(c1 > 0, (here_dp * n_owner + owner_index) * CPD + c1 - 1, -1)

    rows_l = got_l[:, :width]
    ids_l = ids_of(got_l, (here_owner - 1) % n_owner)
    rows_r = got_r[:, :width]
    ids_r = ids_of(got_r, (here_owner + 1) % n_owner)

    def partner_of(ids, owner_index):
        base = (here_dp * n_owner + owner_index) * CPD
        partners = lax.dynamic_slice_in_dim(pair_list, base, CPD)
        local = jnp.clip(ids - base, 0, CPD - 1)
        picked = local[:, None] == jnp.arange(CPD, dtype=jnp.int32)[None, :]
        return jnp.sum(jnp.where(picked, partners[None, :], 0), axis=1)

    def best_against(rows_a, ids_a, partner_a, rows_b, ids_b, itself):
        scores = lax.dot_general(
            rows_a, rows_b, (((1,), (1,)), ((), ())), preferred_element_type=jnp.float32
        )
        same = (ids_a[:, None] == ids_b[None, :]) & (ids_b[None, :] >= 0)
        if itself:
            column = jnp.arange(slots, dtype=jnp.int32)
            same = same & (column[:, None] != column[None, :])
        related = same | (partner_a[:, None] == ids_b[None, :])
        return jnp.max(jnp.where(related, scores, -1.0), axis=1)

    partner = partner_of(mine_ids, here_owner)
    partner_l = partner_of(ids_l, (here_owner - 1) % n_owner)
    far = best_against(rows_l, ids_l, partner_l, rows_r, ids_r, False)
    far_back = lax.ppermute(far, "owner", to_prev)
    best = jnp.maximum(
        jnp.maximum(-1.0, best_against(mine, mine_ids, partner, mine, mine_ids, True)),
        jnp.maximum(
            best_against(mine, mine_ids, partner, rows_l, ids_l, False),
            best_against(mine, mine_ids, partner, rows_r, ids_r, False),
        ),
    )
    best = jnp.maximum(best, far_back)
    wide = jnp.pad(best.reshape(n_dp, capacity), ((0, 0), (0, LANES - capacity)))
    returned = lax.all_to_all(wide, "dp", split_axis=0, concat_axis=0, tiled=True)
    returned = returned[:, :capacity].reshape(slots)
    pick = position[:, None] == jnp.arange(slots, dtype=jnp.int32)[None, :]
    return jnp.sum(jnp.where(pick, returned[None, :], 0.0), axis=1)


def solution(mesh):
    placed = (P(("dp", "owner"), None), P(("dp", "owner")), P())
    return jax.shard_map(
        shards, mesh=mesh, in_specs=placed, out_specs=P(("dp", "owner")), check_vma=False
    )
```

```python
import jax
import jax.numpy as jnp
from jax import lax
from jax.experimental import pallas as pl
from jax.sharding import PartitionSpec as P

CPD = 16
assert CPD & (CPD - 1) == 0
LANES = 128


def _pack_kernel(x_ref, a_ref, out_ref):
    x = x_ref[...].astype(jnp.float32)
    scale = lax.rsqrt(jnp.sum(x * x, axis=1, keepdims=True) + 1e-06)
    width = x.shape[1]
    out_ref[:, :width] = (x * scale).astype(out_ref.dtype)
    code = (jnp.bitwise_and(a_ref[...], CPD - 1) + 1).astype(jnp.float32)
    lane = lax.broadcasted_iota(jnp.int32, (x.shape[0], LANES), 1)
    out_ref[:, width:] = jnp.where(lane == 0, code, 0.0).astype(out_ref.dtype)


def shards(embeddings, assignment, pair_list):
    rows, width = embeddings.shape
    n_dp = lax.axis_size("dp")
    n_owner = lax.axis_size("owner")
    assert n_owner == 4
    capacity = 2 * rows // n_dp
    slots = capacity * n_dp
    here_owner = lax.axis_index("owner")
    here_dp = lax.axis_index("dp")
    target = assignment // (n_owner * CPD)
    onehot = (target[:, None] == jnp.arange(n_dp, dtype=jnp.int32)[None, :]).astype(jnp.int32)
    slot = jnp.sum(jnp.cumsum(onehot, axis=0) * onehot, axis=1) - 1
    position = target * capacity + slot
    first_id = (here_dp * n_owner + here_owner) * CPD

    packed = pl.pallas_call(
        _pack_kernel, out_shape=jax.ShapeDtypeStruct((rows, width + LANES), jnp.bfloat16)
    )(embeddings, assignment.reshape(rows, 1))
    place = (target[None, None, :] == jnp.arange(n_dp, dtype=jnp.int32)[:, None, None]) & (
        slot[None, None, :] == jnp.arange(capacity, dtype=jnp.int32)[None, :, None]
    )
    send = jnp.einsum(
        "tkr,rw->tkw", place.astype(jnp.bfloat16), packed, preferred_element_type=jnp.float32
    ).astype(jnp.bfloat16)
    got = lax.all_to_all(send, "dp", split_axis=0, concat_axis=0, tiled=True).reshape(
        slots, width + LANES
    )

    mine = got[:, :width]
    c1 = got[:, width].astype(jnp.int32)
    mine_ids = jnp.where(c1 > 0, first_id + c1 - 1, -1)

    to_next = [(i, (i + 1) % n_owner) for i in range(n_owner)]
    to_prev = [(i, (i - 1) % n_owner) for i in range(n_owner)]
    got_l = lax.ppermute(got, "owner", to_next)
    got_r = lax.ppermute(got, "owner", to_prev)

    def ids_of(block, owner_index):
        c1 = block[:, width].astype(jnp.int32)
        return jnp.where(c1 > 0, (here_dp * n_owner + owner_index) * CPD + c1 - 1, -1)

    rows_l = got_l[:, :width]
    ids_l = ids_of(got_l, (here_owner - 1) % n_owner)
    rows_r = got_r[:, :width]
    ids_r = ids_of(got_r, (here_owner + 1) % n_owner)

    def partner_of(ids, owner_index):
        base = (here_dp * n_owner + owner_index) * CPD
        partners = lax.dynamic_slice_in_dim(pair_list, base, CPD)
        local = jnp.clip(ids - base, 0, CPD - 1)
        picked = local[:, None] == jnp.arange(CPD, dtype=jnp.int32)[None, :]
        return jnp.sum(jnp.where(picked, partners[None, :], 0), axis=1)

    def best_against(rows_a, ids_a, partner_a, rows_b, ids_b, itself):
        scores = lax.dot_general(
            rows_a, rows_b, (((1,), (1,)), ((), ())), preferred_element_type=jnp.float32
        )
        same = (ids_a[:, None] == ids_b[None, :]) & (ids_b[None, :] >= 0)
        if itself:
            column = jnp.arange(slots, dtype=jnp.int32)
            same = same & (column[:, None] != column[None, :])
        related = same | (partner_a[:, None] == ids_b[None, :])
        return jnp.max(jnp.where(related, scores, -1.0), axis=1)

    partner = partner_of(mine_ids, here_owner)
    partner_l = partner_of(ids_l, (here_owner - 1) % n_owner)
    far = best_against(rows_l, ids_l, partner_l, rows_r, ids_r, False)
    far_back = lax.ppermute(far, "owner", to_prev)
    best = jnp.maximum(
        jnp.maximum(-1.0, best_against(mine, mine_ids, partner, mine, mine_ids, True)),
        jnp.maximum(
            best_against(mine, mine_ids, partner, rows_l, ids_l, False),
            best_against(mine, mine_ids, partner, rows_r, ids_r, False),
        ),
    )
    best = jnp.maximum(best, far_back)
    wide = jnp.pad(best.reshape(n_dp, capacity), ((0, 0), (0, LANES - capacity)))
    returned = lax.all_to_all(wide, "dp", split_axis=0, concat_axis=0, tiled=True)
    returned = returned[:, :capacity].reshape(slots)
    pick = position[:, None] == jnp.arange(slots, dtype=jnp.int32)[None, :]
    return jnp.sum(jnp.where(pick, returned[None, :], 0.0), axis=1)


def solution(mesh):
    placed = (P(("dp", "owner"), None), P(("dp", "owner")), P())
    return jax.shard_map(
        shards, mesh=mesh, in_specs=placed, out_specs=P(("dp", "owner")), check_vma=False
    )
```

```python
import jax
import jax.numpy as jnp
from jax import lax
from jax.sharding import PartitionSpec as P

CPD = 16
LANES = 128


def shards(embeddings, assignment, pair_list):
    rows, width = embeddings.shape
    n_dp = lax.axis_size("dp")
    n_owner = lax.axis_size("owner")
    assert n_owner == 4
    capacity = 2 * rows // n_dp
    slots = capacity * n_dp
    here_owner = lax.axis_index("owner")
    here_dp = lax.axis_index("dp")
    values = embeddings.astype(jnp.float32)
    gram = lax.dot_general(
        embeddings, embeddings, (((1,), (1,)), ((), ())), preferred_element_type=jnp.float32
    )
    order = jnp.arange(rows, dtype=jnp.int32)
    squares = jnp.sum(jnp.where(order[:, None] == order[None, :], gram, 0.0), axis=1)
    unit = (values * lax.rsqrt(squares + 1e-06)[:, None]).astype(jnp.bfloat16)
    target = lax.div(assignment, n_owner * CPD)
    earlier = (target[:, None] == target[None, :]) & (order[None, :] < order[:, None])
    slot = jnp.sum(earlier.astype(jnp.int32), axis=1)
    position = target * capacity + slot
    first_id = (here_dp * n_owner + here_owner) * CPD

    code = (assignment % CPD + 1).astype(jnp.bfloat16)
    lane = jnp.arange(LANES, dtype=jnp.int32)
    extra = jnp.where(lane[None, :] == 0, code[:, None], jnp.zeros((), jnp.bfloat16))
    packed = jnp.concatenate([unit, extra], axis=1)
    place = (target[None, None, :] == jnp.arange(n_dp, dtype=jnp.int32)[:, None, None]) & (
        slot[None, None, :] == jnp.arange(capacity, dtype=jnp.int32)[None, :, None]
    )
    send = jnp.einsum(
        "tkr,rw->tkw", place.astype(jnp.bfloat16), packed, preferred_element_type=jnp.float32
    ).astype(jnp.bfloat16)
    got = lax.all_to_all(send, "dp", split_axis=0, concat_axis=0, tiled=True).reshape(
        slots, width + LANES
    )

    mine = got[:, :width]
    c1 = got[:, width].astype(jnp.int32)
    mine_ids = jnp.where(c1 > 0, first_id + c1 - 1, -1)

    to_next = [(i, (i + 1) % n_owner) for i in range(n_owner)]
    to_prev = [(i, (i - 1) % n_owner) for i in range(n_owner)]
    got_l = lax.ppermute(got, "owner", to_next)
    got_r = lax.ppermute(got, "owner", to_prev)

    def ids_of(block, owner_index):
        c1 = block[:, width].astype(jnp.int32)
        return jnp.where(c1 > 0, (here_dp * n_owner + owner_index) * CPD + c1 - 1, -1)

    rows_l = got_l[:, :width]
    ids_l = ids_of(got_l, (here_owner - 1) % n_owner)
    rows_r = got_r[:, :width]
    ids_r = ids_of(got_r, (here_owner + 1) % n_owner)

    def partner_of(ids, owner_index):
        base = (here_dp * n_owner + owner_index) * CPD
        partners = lax.dynamic_slice_in_dim(pair_list, base, CPD)
        local = jnp.clip(ids - base, 0, CPD - 1)
        picked = local[:, None] == jnp.arange(CPD, dtype=jnp.int32)[None, :]
        return jnp.sum(jnp.where(picked, partners[None, :], 0), axis=1)

    def best_against(rows_a, ids_a, partner_a, rows_b, ids_b, itself):
        scores = lax.dot_general(
            rows_a, rows_b, (((1,), (1,)), ((), ())), preferred_element_type=jnp.float32
        )
        same = (ids_a[:, None] == ids_b[None, :]) & (ids_b[None, :] >= 0)
        if itself:
            column = jnp.arange(slots, dtype=jnp.int32)
            same = same & (column[:, None] != column[None, :])
        related = same | (partner_a[:, None] == ids_b[None, :])
        return jnp.max(jnp.where(related, scores, -1.0), axis=1)

    partner = partner_of(mine_ids, here_owner)
    partner_l = partner_of(ids_l, (here_owner - 1) % n_owner)
    far = best_against(rows_l, ids_l, partner_l, rows_r, ids_r, False)
    best = jnp.maximum(
        jnp.maximum(-1.0, best_against(mine, mine_ids, partner, mine, mine_ids, True)),
        jnp.maximum(
            best_against(mine, mine_ids, partner, rows_l, ids_l, False),
            best_against(mine, mine_ids, partner, rows_r, ids_r, False),
        ),
    )
    wide = jnp.concatenate(
        [best.reshape(n_dp, capacity), far.reshape(n_dp, capacity)], axis=1
    )
    wide = jnp.pad(wide, ((0, 0), (0, LANES - 2 * capacity)))
    returned = lax.all_to_all(wide, "dp", split_axis=0, concat_axis=0, tiled=True)
    far_here = lax.ppermute(returned[:, capacity : 2 * capacity], "owner", to_prev)
    returned = jnp.maximum(returned[:, :capacity], far_here).reshape(slots)
    pick = position[:, None] == jnp.arange(slots, dtype=jnp.int32)[None, :]
    return jnp.sum(jnp.where(pick, returned[None, :], 0.0), axis=1)


def solution(mesh):
    placed = (P(("dp", "owner"), None), P(("dp", "owner")), P())
    return jax.shard_map(
        shards, mesh=mesh, in_specs=placed, out_specs=P(("dp", "owner")), check_vma=False
    )
```

```python
import jax
import jax.numpy as jnp
from jax import lax
from jax.sharding import PartitionSpec as P

CPD = 16
LANES = 128


def shards(embeddings, assignment, pair_list):
    rows, width = embeddings.shape
    n_dp = lax.axis_size("dp")
    n_owner = lax.axis_size("owner")
    assert n_owner == 4
    capacity = 2 * rows // n_dp
    slots = capacity * n_dp
    here_owner = lax.axis_index("owner")
    here_dp = lax.axis_index("dp")
    values = embeddings.astype(jnp.float32)
    gram = lax.dot_general(
        embeddings, embeddings, (((1,), (1,)), ((), ())), preferred_element_type=jnp.float32
    )
    order = jnp.arange(rows, dtype=jnp.int32)
    squares = jnp.sum(jnp.where(order[:, None] == order[None, :], gram, 0.0), axis=1)
    unit = (values * lax.rsqrt(squares + 1e-06)[:, None]).astype(jnp.bfloat16)
    target = lax.div(assignment, n_owner * CPD)
    earlier = (target[:, None] == target[None, :]) & (order[None, :] < order[:, None])
    slot = jnp.sum(earlier.astype(jnp.int32), axis=1)
    position = target * capacity + slot
    first_id = (here_dp * n_owner + here_owner) * CPD

    code = (assignment % CPD + 1).astype(jnp.bfloat16)
    lane = jnp.arange(LANES, dtype=jnp.int32)
    extra = jnp.where(lane[None, :] == 0, code[:, None], jnp.zeros((), jnp.bfloat16))
    packed = jnp.concatenate([unit, extra], axis=1)
    place = (target[None, None, :] == jnp.arange(n_dp, dtype=jnp.int32)[:, None, None]) & (
        slot[None, None, :] == jnp.arange(capacity, dtype=jnp.int32)[None, :, None]
    )
    send = jnp.einsum(
        "tkr,rw->tkw", place.astype(jnp.bfloat16), packed, preferred_element_type=jnp.float32
    ).astype(jnp.bfloat16)
    got = lax.all_to_all(send, "dp", split_axis=0, concat_axis=0, tiled=True).reshape(
        slots, width + LANES
    )

    mine = got[:, :width]
    c1 = got[:, width].astype(jnp.int32)
    mine_ids = jnp.where(c1 > 0, first_id + c1 - 1, -1)

    to_next = [(i, (i + 1) % n_owner) for i in range(n_owner)]
    to_prev = [(i, (i - 1) % n_owner) for i in range(n_owner)]
    got_l = lax.ppermute(got, "owner", to_next)
    got_r = lax.ppermute(got, "owner", to_prev)

    def ids_of(block, owner_index):
        c1 = block[:, width].astype(jnp.int32)
        return jnp.where(c1 > 0, (here_dp * n_owner + owner_index) * CPD + c1 - 1, -1)

    rows_l = got_l[:, :width]
    ids_l = ids_of(got_l, (here_owner - 1) % n_owner)
    rows_r = got_r[:, :width]
    ids_r = ids_of(got_r, (here_owner + 1) % n_owner)

    def partner_of(ids, owner_index):
        base = (here_dp * n_owner + owner_index) * CPD
        partners = lax.dynamic_slice_in_dim(pair_list, base, CPD)
        local = jnp.clip(ids - base, 0, CPD - 1)
        picked = local[:, None] == jnp.arange(CPD, dtype=jnp.int32)[None, :]
        return jnp.sum(jnp.where(picked, partners[None, :], 0), axis=1)

    def best_against(rows_a, ids_a, partner_a, rows_b, ids_b, itself):
        scores = lax.dot_general(
            rows_a, rows_b, (((1,), (1,)), ((), ())), preferred_element_type=jnp.float32
        )
        same = (ids_a[:, None] == ids_b[None, :]) & (ids_b[None, :] >= 0)
        if itself:
            column = jnp.arange(slots, dtype=jnp.int32)
            same = same & (column[:, None] != column[None, :])
        related = same | (partner_a[:, None] == ids_b[None, :])
        return jnp.max(jnp.where(related, scores, -1.0), axis=1)

    partner = partner_of(mine_ids, here_owner)
    partner_l = partner_of(ids_l, (here_owner - 1) % n_owner)
    far = best_against(rows_l, ids_l, partner_l, rows_r, ids_r, False)
    far_back = lax.ppermute(far, "owner", to_prev)
    best = jnp.maximum(
        jnp.maximum(-1.0, best_against(mine, mine_ids, partner, mine, mine_ids, True)),
        jnp.maximum(
            best_against(mine, mine_ids, partner, rows_l, ids_l, False),
            best_against(mine, mine_ids, partner, rows_r, ids_r, False),
        ),
    )
    best = jnp.maximum(best, far_back)
    wide = jnp.pad(best.reshape(n_dp, capacity), ((0, 0), (0, LANES - capacity)))
    returned = lax.all_to_all(wide, "dp", split_axis=0, concat_axis=0, tiled=True)
    returned = returned[:, :capacity].reshape(slots)
    pick = position[:, None] == jnp.arange(slots, dtype=jnp.int32)[None, :]
    return jnp.sum(jnp.where(pick, returned[None, :], 0.0), axis=1)


def solution(mesh):
    placed = (P(("dp", "owner"), None), P(("dp", "owner")), P())
    return jax.shard_map(
        shards, mesh=mesh, in_specs=placed, out_specs=P(("dp", "owner")), check_vma=False
    )
```

```python
import jax
import jax.numpy as jnp
from jax import lax
from jax.sharding import PartitionSpec as P

CPD = 16
LANES = 128


def shards(embeddings, assignment, pair_list):
    rows, width = embeddings.shape
    n_dp = lax.axis_size("dp")
    n_owner = lax.axis_size("owner")
    assert n_owner == 4
    capacity = 2 * rows // n_dp
    slots = capacity * n_dp
    assert slots <= width
    here_owner = lax.axis_index("owner")
    here_dp = lax.axis_index("dp")
    values = embeddings.astype(jnp.float32)
    gram = lax.dot_general(
        embeddings, embeddings, (((1,), (1,)), ((), ())), preferred_element_type=jnp.float32
    )
    order = jnp.arange(rows, dtype=jnp.int32)
    squares = jnp.sum(jnp.where(order[:, None] == order[None, :], gram, 0.0), axis=1)
    unit = (values * lax.rsqrt(squares + 1e-06)[:, None]).astype(jnp.bfloat16)
    target = lax.div(assignment, n_owner * CPD)
    earlier = (target[:, None] == target[None, :]) & (order[None, :] < order[:, None])
    slot = jnp.sum(earlier.astype(jnp.int32), axis=1)
    position = target * capacity + slot
    first_id = (here_dp * n_owner + here_owner) * CPD

    code = (assignment % CPD + 1).astype(jnp.bfloat16)
    lane = jnp.arange(LANES, dtype=jnp.int32)
    extra = jnp.where(lane[None, :] == 0, code[:, None], jnp.zeros((), jnp.bfloat16))
    packed = jnp.concatenate([unit, extra], axis=1)
    place = (target[None, None, :] == jnp.arange(n_dp, dtype=jnp.int32)[:, None, None]) & (
        slot[None, None, :] == jnp.arange(capacity, dtype=jnp.int32)[None, :, None]
    )
    send = jnp.einsum(
        "tkr,rw->tkw", place.astype(jnp.bfloat16), packed, preferred_element_type=jnp.float32
    ).astype(jnp.bfloat16)
    got = lax.all_to_all(send, "dp", split_axis=0, concat_axis=0, tiled=True).reshape(
        slots, width + LANES
    )

    mine = got[:, :width]
    c1 = got[:, width].astype(jnp.int32)
    mine_ids = jnp.where(c1 > 0, first_id + c1 - 1, -1)

    to_next = [(i, (i + 1) % n_owner) for i in range(n_owner)]
    to_prev = [(i, (i - 1) % n_owner) for i in range(n_owner)]
    code_rows = jnp.pad(got[:, width].reshape(1, slots), ((0, 15), (0, width - slots)))
    block = jnp.concatenate([mine, code_rows], axis=0)
    got_l = lax.ppermute(block, "owner", to_next)
    got_r = lax.ppermute(block, "owner", to_prev)

    def ids_of(block, owner_index):
        c1 = block[slots, :slots].astype(jnp.int32)
        return jnp.where(c1 > 0, (here_dp * n_owner + owner_index) * CPD + c1 - 1, -1)

    rows_l = got_l[:slots]
    ids_l = ids_of(got_l, (here_owner - 1) % n_owner)
    rows_r = got_r[:slots]
    ids_r = ids_of(got_r, (here_owner + 1) % n_owner)

    def partner_of(ids, owner_index):
        base = (here_dp * n_owner + owner_index) * CPD
        partners = lax.dynamic_slice_in_dim(pair_list, base, CPD)
        local = jnp.clip(ids - base, 0, CPD - 1)
        picked = local[:, None] == jnp.arange(CPD, dtype=jnp.int32)[None, :]
        return jnp.sum(jnp.where(picked, partners[None, :], 0), axis=1)

    def best_against(rows_a, ids_a, partner_a, rows_b, ids_b, itself):
        scores = lax.dot_general(
            rows_a, rows_b, (((1,), (1,)), ((), ())), preferred_element_type=jnp.float32
        )
        same = (ids_a[:, None] == ids_b[None, :]) & (ids_b[None, :] >= 0)
        if itself:
            column = jnp.arange(slots, dtype=jnp.int32)
            same = same & (column[:, None] != column[None, :])
        related = same | (partner_a[:, None] == ids_b[None, :])
        return jnp.max(jnp.where(related, scores, -1.0), axis=1)

    partner = partner_of(mine_ids, here_owner)
    partner_l = partner_of(ids_l, (here_owner - 1) % n_owner)
    far = best_against(rows_l, ids_l, partner_l, rows_r, ids_r, False)
    far_back = lax.ppermute(far, "owner", to_prev)
    best = jnp.maximum(
        jnp.maximum(-1.0, best_against(mine, mine_ids, partner, mine, mine_ids, True)),
        jnp.maximum(
            best_against(mine, mine_ids, partner, rows_l, ids_l, False),
            best_against(mine, mine_ids, partner, rows_r, ids_r, False),
        ),
    )
    best = jnp.maximum(best, far_back)
    wide = jnp.pad(best.reshape(n_dp, capacity), ((0, 0), (0, LANES - capacity)))
    returned = lax.all_to_all(wide, "dp", split_axis=0, concat_axis=0, tiled=True)
    returned = returned[:, :capacity].reshape(slots)
    pick = position[:, None] == jnp.arange(slots, dtype=jnp.int32)[None, :]
    return jnp.sum(jnp.where(pick, returned[None, :], 0.0), axis=1)


def solution(mesh):
    placed = (P(("dp", "owner"), None), P(("dp", "owner")), P())
    return jax.shard_map(
        shards, mesh=mesh, in_specs=placed, out_specs=P(("dp", "owner")), check_vma=False
    )
```

```python
import jax
import jax.numpy as jnp
from jax import lax
from jax.sharding import PartitionSpec as P

CPD = 16
LANES = 128


def shards(embeddings, assignment, pair_list):
    rows, width = embeddings.shape
    n_dp = lax.axis_size("dp")
    n_owner = lax.axis_size("owner")
    assert n_owner == 4
    capacity = 2 * rows // n_dp
    slots = capacity * n_dp
    assert slots <= width
    here_owner = lax.axis_index("owner")
    here_dp = lax.axis_index("dp")
    values = embeddings.astype(jnp.float32)
    gram = lax.dot_general(
        embeddings, embeddings, (((1,), (1,)), ((), ())), preferred_element_type=jnp.float32
    )
    order = jnp.arange(rows, dtype=jnp.int32)
    squares = jnp.sum(jnp.where(order[:, None] == order[None, :], gram, 0.0), axis=1)
    unit = (values * lax.rsqrt(squares + 1e-06)[:, None]).astype(jnp.bfloat16)
    target = lax.div(assignment, n_owner * CPD)
    earlier = (target[:, None] == target[None, :]) & (order[None, :] < order[:, None])
    slot = jnp.sum(earlier.astype(jnp.int32), axis=1)
    position = target * capacity + slot
    first_id = (here_dp * n_owner + here_owner) * CPD

    code = (assignment % CPD + 1).astype(jnp.bfloat16)
    lane = jnp.arange(LANES, dtype=jnp.int32)
    extra = jnp.where(lane[None, :] == 0, code[:, None], jnp.zeros((), jnp.bfloat16))
    packed = jnp.concatenate([unit, extra], axis=1)
    place = (target[None, None, :] == jnp.arange(n_dp, dtype=jnp.int32)[:, None, None]) & (
        slot[None, None, :] == jnp.arange(capacity, dtype=jnp.int32)[None, :, None]
    )
    send = jnp.einsum(
        "tkr,rw->tkw", place.astype(jnp.bfloat16), packed, preferred_element_type=jnp.float32
    ).astype(jnp.bfloat16)
    to_next = [(i, (i + 1) % n_owner) for i in range(n_owner)]
    to_prev = [(i, (i - 1) % n_owner) for i in range(n_owner)]
    warm = (
        lax.ppermute(assignment[:8], "owner", to_next),
        lax.ppermute(assignment[:8], "owner", to_prev),
    )
    got = lax.all_to_all(send, "dp", split_axis=0, concat_axis=0, tiled=True).reshape(
        slots, width + LANES
    )
    first_id = jnp.where(warm[0][0] + warm[1][0] < 0, 0, first_id)

    mine = got[:, :width]
    c1 = got[:, width].astype(jnp.int32)
    mine_ids = jnp.where(c1 > 0, first_id + c1 - 1, -1)

    code_rows = jnp.pad(got[:, width].reshape(1, slots), ((0, 15), (0, width - slots)))
    block = jnp.concatenate([mine, code_rows], axis=0)
    got_l = lax.ppermute(block, "owner", to_next)
    got_r = lax.ppermute(block, "owner", to_prev)

    def ids_of(block, owner_index):
        c1 = block[slots, :slots].astype(jnp.int32)
        return jnp.where(c1 > 0, (here_dp * n_owner + owner_index) * CPD + c1 - 1, -1)

    rows_l = got_l[:slots]
    ids_l = ids_of(got_l, (here_owner - 1) % n_owner)
    rows_r = got_r[:slots]
    ids_r = ids_of(got_r, (here_owner + 1) % n_owner)

    def partner_of(ids, owner_index):
        base = (here_dp * n_owner + owner_index) * CPD
        partners = lax.dynamic_slice_in_dim(pair_list, base, CPD)
        local = jnp.clip(ids - base, 0, CPD - 1)
        picked = local[:, None] == jnp.arange(CPD, dtype=jnp.int32)[None, :]
        return jnp.sum(jnp.where(picked, partners[None, :], 0), axis=1)

    def best_against(rows_a, ids_a, partner_a, rows_b, ids_b, itself):
        scores = lax.dot_general(
            rows_a, rows_b, (((1,), (1,)), ((), ())), preferred_element_type=jnp.float32
        )
        same = (ids_a[:, None] == ids_b[None, :]) & (ids_b[None, :] >= 0)
        if itself:
            column = jnp.arange(slots, dtype=jnp.int32)
            same = same & (column[:, None] != column[None, :])
        related = same | (partner_a[:, None] == ids_b[None, :])
        return jnp.max(jnp.where(related, scores, -1.0), axis=1)

    partner = partner_of(mine_ids, here_owner)
    partner_l = partner_of(ids_l, (here_owner - 1) % n_owner)
    far = best_against(rows_l, ids_l, partner_l, rows_r, ids_r, False)
    far_back = lax.ppermute(far, "owner", to_prev)
    best = jnp.maximum(
        jnp.maximum(-1.0, best_against(mine, mine_ids, partner, mine, mine_ids, True)),
        jnp.maximum(
            best_against(mine, mine_ids, partner, rows_l, ids_l, False),
            best_against(mine, mine_ids, partner, rows_r, ids_r, False),
        ),
    )
    best = jnp.maximum(best, far_back)
    wide = jnp.pad(best.reshape(n_dp, capacity), ((0, 0), (0, LANES - capacity)))
    returned = lax.all_to_all(wide, "dp", split_axis=0, concat_axis=0, tiled=True)
    returned = returned[:, :capacity].reshape(slots)
    pick = position[:, None] == jnp.arange(slots, dtype=jnp.int32)[None, :]
    return jnp.sum(jnp.where(pick, returned[None, :], 0.0), axis=1)


def solution(mesh):
    placed = (P(("dp", "owner"), None), P(("dp", "owner")), P())
    return jax.shard_map(
        shards, mesh=mesh, in_specs=placed, out_specs=P(("dp", "owner")), check_vma=False
    )
```

```python
import jax
import jax.numpy as jnp
from jax import lax
from jax.sharding import PartitionSpec as P

CPD = 16
LANES = 128


def shards(embeddings, assignment, pair_list):
    rows, width = embeddings.shape
    n_dp = lax.axis_size("dp")
    n_owner = lax.axis_size("owner")
    assert n_owner == 4
    capacity = 2 * rows // n_dp
    slots = capacity * n_dp
    assert slots <= width
    here_owner = lax.axis_index("owner")
    here_dp = lax.axis_index("dp")
    values = embeddings.astype(jnp.float32)
    gram = lax.dot_general(
        embeddings, embeddings, (((1,), (1,)), ((), ())), preferred_element_type=jnp.float32
    )
    order = jnp.arange(rows, dtype=jnp.int32)
    squares = jnp.sum(jnp.where(order[:, None] == order[None, :], gram, 0.0), axis=1)
    unit = (values * lax.rsqrt(squares + 1e-06)[:, None]).astype(jnp.bfloat16)
    target = lax.div(assignment, n_owner * CPD)
    earlier = (target[:, None] == target[None, :]) & (order[None, :] < order[:, None])
    slot = jnp.sum(earlier.astype(jnp.int32), axis=1)
    position = target * capacity + slot
    first_id = (here_dp * n_owner + here_owner) * CPD

    code = (assignment % CPD + 1).astype(jnp.bfloat16)
    lane = jnp.arange(LANES, dtype=jnp.int32)
    extra = jnp.where(lane[None, :] == 0, code[:, None], jnp.zeros((), jnp.bfloat16))
    packed = jnp.concatenate([unit, extra], axis=1)
    place = (target[None, None, :] == jnp.arange(n_dp, dtype=jnp.int32)[:, None, None]) & (
        slot[None, None, :] == jnp.arange(capacity, dtype=jnp.int32)[None, :, None]
    )
    send = jnp.einsum(
        "tkr,rw->tkw", place.astype(jnp.bfloat16), packed, preferred_element_type=jnp.float32
    ).astype(jnp.bfloat16)
    got = lax.all_to_all(send, "dp", split_axis=0, concat_axis=0, tiled=True).reshape(
        slots, width + LANES
    )

    mine = got[:, :width]
    c1 = got[:, width].astype(jnp.int32)
    mine_ids = jnp.where(c1 > 0, first_id + c1 - 1, -1)

    to_next = [(i, (i + 1) % n_owner) for i in range(n_owner)]
    to_prev = [(i, (i - 1) % n_owner) for i in range(n_owner)]
    code_rows = jnp.pad(got[:, width].reshape(1, slots), ((0, 15), (0, width - slots)))
    block = jnp.concatenate([mine, code_rows], axis=0)
    got_l = lax.ppermute(block, "owner", to_next)
    got_r = lax.ppermute(block, "owner", to_prev)

    def ids_of(block, owner_index):
        c1 = block[slots, :slots].astype(jnp.int32)
        return jnp.where(c1 > 0, (here_dp * n_owner + owner_index) * CPD + c1 - 1, -1)

    rows_l = got_l[:slots]
    ids_l = ids_of(got_l, (here_owner - 1) % n_owner)
    rows_r = got_r[:slots]
    ids_r = ids_of(got_r, (here_owner + 1) % n_owner)

    def partner_of(ids, owner_index):
        base = (here_dp * n_owner + owner_index) * CPD
        partners = lax.dynamic_slice_in_dim(pair_list, base, CPD)
        local = jnp.clip(ids - base, 0, CPD - 1)
        picked = local[:, None] == jnp.arange(CPD, dtype=jnp.int32)[None, :]
        return jnp.sum(jnp.where(picked, partners[None, :], 0), axis=1)

    def best_against(rows_a, ids_a, partner_a, rows_b, ids_b, itself):
        scores = lax.dot_general(
            rows_a, rows_b, (((1,), (1,)), ((), ())), preferred_element_type=jnp.float32
        )
        same = (ids_a[:, None] == ids_b[None, :]) & (ids_b[None, :] >= 0)
        if itself:
            column = jnp.arange(slots, dtype=jnp.int32)
            same = same & (column[:, None] != column[None, :])
        related = same | (partner_a[:, None] == ids_b[None, :])
        return jnp.max(jnp.where(related, scores, -1.0), axis=1)

    partner = partner_of(mine_ids, here_owner)
    partner_l = partner_of(ids_l, (here_owner - 1) % n_owner)
    far = best_against(rows_l, ids_l, partner_l, rows_r, ids_r, False)
    far_back = lax.ppermute(far, "owner", to_prev)
    best = jnp.maximum(
        jnp.maximum(-1.0, best_against(mine, mine_ids, partner, mine, mine_ids, True)),
        jnp.maximum(
            best_against(mine, mine_ids, partner, rows_l, ids_l, False),
            best_against(mine, mine_ids, partner, rows_r, ids_r, False),
        ),
    )
    best = jnp.maximum(best, far_back)
    wide = jnp.pad(best.reshape(n_dp, capacity), ((0, 0), (0, LANES - capacity)))
    returned = lax.all_to_all(wide, "dp", split_axis=0, concat_axis=0, tiled=True)
    returned = returned[:, :capacity].reshape(slots)
    pick = (position[:, None] == jnp.arange(slots, dtype=jnp.int32)[None, :]).astype(jnp.float32)
    return jnp.dot(pick, returned, precision=lax.Precision.HIGHEST)


def solution(mesh):
    placed = (P(("dp", "owner"), None), P(("dp", "owner")), P())
    return jax.shard_map(
        shards, mesh=mesh, in_specs=placed, out_specs=P(("dp", "owner")), check_vma=False
    )
```

```python
import jax
import jax.numpy as jnp
from jax import lax
from jax.sharding import PartitionSpec as P

CPD = 16
LANES = 128


def shards(embeddings, assignment, pair_list):
    rows, width = embeddings.shape
    n_dp = lax.axis_size("dp")
    n_owner = lax.axis_size("owner")
    assert n_owner == 4
    capacity = 2 * rows // n_dp
    slots = capacity * n_dp
    assert slots <= width and rows <= LANES
    here_owner = lax.axis_index("owner")
    here_dp = lax.axis_index("dp")
    values = embeddings.astype(jnp.float32)
    gram = lax.dot_general(
        embeddings, embeddings, (((1,), (1,)), ((), ())), preferred_element_type=jnp.float32
    )
    order = jnp.arange(rows, dtype=jnp.int32)
    squares = jnp.sum(jnp.where(order[:, None] == order[None, :], gram, 0.0), axis=1)
    unit = (values * lax.rsqrt(squares + 1e-06)[:, None]).astype(jnp.bfloat16)
    target = lax.div(assignment, n_owner * CPD)
    earlier = (target[:, None] == target[None, :]) & (order[None, :] < order[:, None])
    slot = jnp.sum(earlier.astype(jnp.int32), axis=1)
    position = target * capacity + slot
    first_id = (here_dp * n_owner + here_owner) * CPD

    code = (assignment % CPD + 1).astype(jnp.bfloat16)
    lane = jnp.arange(LANES, dtype=jnp.int32)
    row_index = jnp.arange(rows, dtype=jnp.int32).astype(jnp.bfloat16)
    extra = jnp.where(
        lane[None, :] == 0,
        code[:, None],
        jnp.where(lane[None, :] == 1, row_index[:, None], jnp.zeros((), jnp.bfloat16)),
    )
    packed = jnp.concatenate([unit, extra], axis=1)
    place = (target[None, None, :] == jnp.arange(n_dp, dtype=jnp.int32)[:, None, None]) & (
        slot[None, None, :] == jnp.arange(capacity, dtype=jnp.int32)[None, :, None]
    )
    send = jnp.einsum(
        "tkr,rw->tkw", place.astype(jnp.bfloat16), packed, preferred_element_type=jnp.float32
    ).astype(jnp.bfloat16)
    got = lax.all_to_all(send, "dp", split_axis=0, concat_axis=0, tiled=True).reshape(
        slots, width + LANES
    )

    mine = got[:, :width]
    c1 = got[:, width].astype(jnp.int32)
    mine_ids = jnp.where(c1 > 0, first_id + c1 - 1, -1)

    to_next = [(i, (i + 1) % n_owner) for i in range(n_owner)]
    to_prev = [(i, (i - 1) % n_owner) for i in range(n_owner)]
    code_rows = jnp.pad(got[:, width].reshape(1, slots), ((0, 15), (0, width - slots)))
    block = jnp.concatenate([mine, code_rows], axis=0)
    got_l = lax.ppermute(block, "owner", to_next)
    got_r = lax.ppermute(block, "owner", to_prev)

    def ids_of(block, owner_index):
        c1 = block[slots, :slots].astype(jnp.int32)
        return jnp.where(c1 > 0, (here_dp * n_owner + owner_index) * CPD + c1 - 1, -1)

    rows_l = got_l[:slots]
    ids_l = ids_of(got_l, (here_owner - 1) % n_owner)
    rows_r = got_r[:slots]
    ids_r = ids_of(got_r, (here_owner + 1) % n_owner)

    def partner_of(ids, owner_index):
        base = (here_dp * n_owner + owner_index) * CPD
        partners = lax.dynamic_slice_in_dim(pair_list, base, CPD)
        local = jnp.clip(ids - base, 0, CPD - 1)
        picked = local[:, None] == jnp.arange(CPD, dtype=jnp.int32)[None, :]
        return jnp.sum(jnp.where(picked, partners[None, :], 0), axis=1)

    def best_against(rows_a, ids_a, partner_a, rows_b, ids_b, itself):
        scores = lax.dot_general(
            rows_a, rows_b, (((1,), (1,)), ((), ())), preferred_element_type=jnp.float32
        )
        same = (ids_a[:, None] == ids_b[None, :]) & (ids_b[None, :] >= 0)
        if itself:
            column = jnp.arange(slots, dtype=jnp.int32)
            same = same & (column[:, None] != column[None, :])
        related = same | (partner_a[:, None] == ids_b[None, :])
        return jnp.max(jnp.where(related, scores, -1.0), axis=1)

    partner = partner_of(mine_ids, here_owner)
    partner_l = partner_of(ids_l, (here_owner - 1) % n_owner)
    far = best_against(rows_l, ids_l, partner_l, rows_r, ids_r, False)
    far_back = lax.ppermute(far, "owner", to_prev)
    best = jnp.maximum(
        jnp.maximum(-1.0, best_against(mine, mine_ids, partner, mine, mine_ids, True)),
        jnp.maximum(
            best_against(mine, mine_ids, partner, rows_l, ids_l, False),
            best_against(mine, mine_ids, partner, rows_r, ids_r, False),
        ),
    )
    best = jnp.maximum(best, far_back)
    source_row = got[:, width + 1].astype(jnp.int32).reshape(n_dp, capacity, 1)
    filled = (c1 > 0).reshape(n_dp, capacity, 1)
    at_row = filled & (source_row == jnp.arange(LANES, dtype=jnp.int32)[None, None, :])
    wide = jnp.max(jnp.where(at_row, best.reshape(n_dp, capacity, 1), -2.0), axis=1)
    returned = lax.all_to_all(wide, "dp", split_axis=0, concat_axis=0, tiled=True)
    return jnp.max(returned[:, :rows], axis=0)


def solution(mesh):
    placed = (P(("dp", "owner"), None), P(("dp", "owner")), P())
    return jax.shard_map(
        shards, mesh=mesh, in_specs=placed, out_specs=P(("dp", "owner")), check_vma=False
    )
```

```python
import jax
import jax.numpy as jnp
from jax import lax
from jax.sharding import PartitionSpec as P

CPD = 16
assert CPD & (CPD - 1) == 0
LANES = 128


def shards(embeddings, assignment, pair_list):
    rows, width = embeddings.shape
    n_dp = lax.axis_size("dp")
    n_owner = lax.axis_size("owner")
    assert n_owner == 4
    capacity = 2 * rows // n_dp
    slots = capacity * n_dp
    assert slots <= width and rows <= LANES
    here_owner = lax.axis_index("owner")
    here_dp = lax.axis_index("dp")
    values = embeddings.astype(jnp.float32)
    gram = lax.dot_general(
        embeddings, embeddings, (((1,), (1,)), ((), ())), preferred_element_type=jnp.float32
    )
    order = jnp.arange(rows, dtype=jnp.int32)
    squares = jnp.sum(jnp.where(order[:, None] == order[None, :], gram, 0.0), axis=1)
    unit = (values * lax.rsqrt(squares + 1e-06)[:, None]).astype(jnp.bfloat16)
    group = n_owner * CPD
    assert group & (group - 1) == 0
    target = lax.shift_right_logical(assignment, group.bit_length() - 1)
    earlier = (target[:, None] == target[None, :]) & (order[None, :] < order[:, None])
    slot = jnp.sum(earlier.astype(jnp.int32), axis=1)
    position = target * capacity + slot
    first_id = (here_dp * n_owner + here_owner) * CPD

    code = (jnp.bitwise_and(assignment, CPD - 1) + 1).astype(jnp.bfloat16)
    lane = jnp.arange(LANES, dtype=jnp.int32)
    row_index = jnp.arange(rows, dtype=jnp.int32).astype(jnp.bfloat16)
    extra = jnp.where(
        lane[None, :] == 0,
        code[:, None],
        jnp.where(lane[None, :] == 1, row_index[:, None], jnp.zeros((), jnp.bfloat16)),
    )
    packed = jnp.concatenate([unit, extra], axis=1)
    place = (target[None, None, :] == jnp.arange(n_dp, dtype=jnp.int32)[:, None, None]) & (
        slot[None, None, :] == jnp.arange(capacity, dtype=jnp.int32)[None, :, None]
    )
    send = jnp.einsum(
        "tkr,rw->tkw", place.astype(jnp.bfloat16), packed, preferred_element_type=jnp.float32
    ).astype(jnp.bfloat16)
    got = lax.all_to_all(send, "dp", split_axis=0, concat_axis=0, tiled=True).reshape(
        slots, width + LANES
    )

    mine = got[:, :width]
    c1 = got[:, width].astype(jnp.int32)
    mine_ids = jnp.where(c1 > 0, first_id + c1 - 1, -1)

    to_next = [(i, (i + 1) % n_owner) for i in range(n_owner)]
    to_prev = [(i, (i - 1) % n_owner) for i in range(n_owner)]
    code_rows = jnp.pad(got[:, width].reshape(1, slots), ((0, 15), (0, width - slots)))
    block = jnp.concatenate([mine, code_rows], axis=0)
    got_l = lax.ppermute(block, "owner", to_next)
    got_r = lax.ppermute(block, "owner", to_prev)

    def ids_of(block, owner_index):
        c1 = block[slots, :slots].astype(jnp.int32)
        return jnp.where(c1 > 0, (here_dp * n_owner + owner_index) * CPD + c1 - 1, -1)

    rows_l = got_l[:slots]
    ids_l = ids_of(got_l, (here_owner - 1) % n_owner)
    rows_r = got_r[:slots]
    ids_r = ids_of(got_r, (here_owner + 1) % n_owner)

    def partner_of(ids, owner_index):
        base = (here_dp * n_owner + owner_index) * CPD
        partners = lax.dynamic_slice_in_dim(pair_list, base, CPD)
        local = jnp.clip(ids - base, 0, CPD - 1)
        picked = local[:, None] == jnp.arange(CPD, dtype=jnp.int32)[None, :]
        return jnp.sum(jnp.where(picked, partners[None, :], 0), axis=1)

    def best_against(rows_a, ids_a, partner_a, rows_b, ids_b, itself):
        scores = lax.dot_general(
            rows_a, rows_b, (((1,), (1,)), ((), ())), preferred_element_type=jnp.float32
        )
        same = (ids_a[:, None] == ids_b[None, :]) & (ids_b[None, :] >= 0)
        if itself:
            column = jnp.arange(slots, dtype=jnp.int32)
            same = same & (column[:, None] != column[None, :])
        related = same | (partner_a[:, None] == ids_b[None, :])
        return jnp.max(jnp.where(related, scores, -1.0), axis=1)

    partner = partner_of(mine_ids, here_owner)
    partner_l = partner_of(ids_l, (here_owner - 1) % n_owner)
    far = best_against(rows_l, ids_l, partner_l, rows_r, ids_r, False)
    far_back = lax.ppermute(far, "owner", to_prev)
    best = jnp.maximum(
        jnp.maximum(-1.0, best_against(mine, mine_ids, partner, mine, mine_ids, True)),
        jnp.maximum(
            best_against(mine, mine_ids, partner, rows_l, ids_l, False),
            best_against(mine, mine_ids, partner, rows_r, ids_r, False),
        ),
    )
    best = jnp.maximum(best, far_back)
    source_row = got[:, width + 1].astype(jnp.int32).reshape(n_dp, capacity, 1)
    filled = (c1 > 0).reshape(n_dp, capacity, 1)
    at_row = filled & (source_row == jnp.arange(LANES, dtype=jnp.int32)[None, None, :])
    wide = jnp.max(jnp.where(at_row, best.reshape(n_dp, capacity, 1), -2.0), axis=1)
    returned = lax.all_to_all(wide, "dp", split_axis=0, concat_axis=0, tiled=True)
    return jnp.max(returned[:, :rows], axis=0)


def solution(mesh):
    placed = (P(("dp", "owner"), None), P(("dp", "owner")), P())
    return jax.shard_map(
        shards, mesh=mesh, in_specs=placed, out_specs=P(("dp", "owner")), check_vma=False
    )
```
